768 devices in a mesh: lat: 48 (over z_lo, x, core), lon: 16 (over y, z_hi).
Axes of the slice: x: 4, y: 8, z: 12 (z_hi: 2, z_lo: 6; z = z_hi * 6 + z_lo), core: 2. Of those that a mesh axis runs over, the one named last changes fastest.
Arguments:
- tracers: float32 [3, 1, 768, 6144], P(None, None, 'lat', 'lon'), may hold values from -6 to 6
- lon_offsets: int32 [768], P('lat'), may hold values from -190 to 190, as said below
- lon_weights: float32 [4, 768], P(None, 'lat'), may hold values from -0.25 to 0.75
- lat_offsets: int32 [768], replicated, may hold values from -4 to 4, as said below
- lat_weights: float32 [4, 768], replicated, may hold values from -0.25 to 0.75
Outputs:
- advected: float32 [3, 1, 768, 6144], P(None, None, 'lat', 'lon')
The draws below stay inside these ranges and needn't reach their ends.
Inputs may be any that keep to these rules, and one draw needn't show every extreme that they name: `lon_offsets`: magnitudes are larger in the polar quarters of the rows; the bound is reached in every draw. `lat_offsets`: the bound is reached in every draw.
All inputs are finite; a program needn't handle non-finite values.
Results may differ from the reference program's by a relative error of at most 0.0003.
Values sent between devices are 32-bit elements; how exact they have to be, the bound alone decides.
No kernel may reach another device: no remote copies, remote signals or barrier semaphores. Data moves between devices by JAX's collectives and lax.ppermute only.
A program may use at most 64 MiB of HBM per device.

```python
import jax
import jax.numpy as jnp
from jax import lax

TRACERS = 3
LEVELS = 1
NLAT = 768
NLON = 6144
HALO = 192
LATH = 6


def draw_lon_offsets(key, part):
    rows = jnp.arange(NLAT, dtype=jnp.int32)
    distance = jnp.minimum(rows, NLAT - 1 - rows)
    quarter = NLAT // 4
    reach = 2 + (HALO - 4) * jnp.maximum(0, quarter - distance) // quarter
    drawn = jax.random.randint(key, (NLAT,), 0, 1 << 20, dtype=jnp.int32)
    offsets = drawn % (2 * reach + 1) - reach
    offsets = offsets.at[0].set(HALO - 2).at[NLAT - 1].set(2 - HALO)
    return offsets.astype(jnp.int32)


def draw_lat_offsets(key, part):
    reach = LATH - 2
    drawn = jax.random.randint(jax.random.fold_in(key, 7), (NLAT,), 0, 1 << 20, dtype=jnp.int32)
    offsets = drawn % (2 * reach + 1) - reach
    middle = NLAT // 2
    offsets = offsets.at[middle].set(reach).at[middle + 1].set(-reach)
    return offsets.astype(jnp.int32)


def levels(rng, extent, cuts, smallest, high):
    gain = 1.0
    for dim, parts in cuts:
        steps = jax.random.uniform(jax.random.fold_in(jax.random.fold_in(rng, 6), dim), (parts,), jnp.float32, smallest / len(cuts), high / len(cuts))
        gain = gain * jnp.repeat(jnp.exp(steps), extent[dim] // parts).reshape((-1,) + (1,) * (len(extent) - 1 - dim))
    return gain


def gaussian(key, extent, scale, most, cuts=(), kind=jnp.bfloat16):
    entries = scale * jax.random.normal(key, extent, jnp.float32)
    if cuts:
        entries = entries * levels(key, extent, cuts, -0.22, 0.18)
    return jnp.clip(entries, -most, most).astype(kind)


def setup_inputs(seed: int = 0) -> dict:
    keys = jax.random.split(jax.random.key(seed), 6)
    tracers = gaussian(keys[0], (TRACERS, LEVELS, NLAT, NLON), 1.0, 6.0, ((2, 48), (3, 16)), jnp.float32)
    lon_offsets = draw_lon_offsets(jax.random.fold_in(keys[5], 71), 0)
    lon_weights = jnp.clip(-0.25 + 1.0 * jax.random.uniform(keys[2], (4, NLAT), jnp.float32) ** levels(keys[2], (4, NLAT), ((1, 48),), -0.2, 0.2), -0.25, 0.75)
    lat_offsets = draw_lat_offsets(jax.random.fold_in(keys[5], 71), 0)
    lat_weights = jnp.clip(jax.random.uniform(keys[4], (4, NLAT), jnp.float32, -0.25, 0.75), -0.25, 0.75)
    return {"tracers": tracers, "lon_offsets": lon_offsets, "lon_weights": lon_weights, "lat_offsets": lat_offsets, "lat_weights": lat_weights}


def row_taps(row, shift, taps, base, length):
    total = jnp.zeros(row.shape[:-1] + (length,), jnp.float32)
    for k in range(4):
        start = (base - shift - 1 + k).astype(jnp.int32)
        total = total + taps[k] * lax.dynamic_slice_in_dim(row, start, length, axis=row.ndim - 1)
    return total


def reference(tracers, lon_offsets, lon_weights, lat_offsets, lat_weights):
    nlat = tracers.shape[2]
    nlon = tracers.shape[3]
    fields = tracers.reshape((-1, nlat, nlon))

    def one_field(field):
        padded = jnp.concatenate([field[:, nlon - HALO:], field, field[:, :HALO]], axis=1)
        swept = jax.vmap(lambda r, s, w: row_taps(r, s, w, HALO, nlon), in_axes=(0, 0, 1))(padded, lon_offsets, lon_weights)
        rows = jnp.arange(nlat, dtype=jnp.int32)
        total = jnp.zeros((nlat, nlon), jnp.float32)
        for k in range(4):
            source = jnp.clip(rows - lat_offsets - 1 + k, 0, nlat - 1).astype(jnp.int32)
            total = total + lat_weights[k][:, None] * jnp.take(swept, source, axis=0)
        return total

    result = lax.map(one_field, fields)
    return result.reshape(tracers.shape)
```

```python
import jax
import jax.numpy as jnp
from jax import lax
from jax.experimental import pallas as pl
from jax.experimental.pallas import tpu as pltpu
from jax.sharding import PartitionSpec as P

LON_HALO = 256
LAT_HALO = 8
SHIFT_BITS = 9
INTERPRET = False


def lon_kernel(left_ref, mid_ref, right_ref, base_ref, w_ref, out_ref, top_ref, bot_ref):
    tracers, rows, width = mid_ref.shape
    ext_width = width + 2 * LON_HALO
    base = base_ref[...]
    masks = [((base >> b) & 1) == 1 for b in range(SHIFT_BITS)]
    w = w_ref[...]
    for t in range(tracers):
        row = jnp.concatenate([left_ref[t], mid_ref[t], right_ref[t]], axis=1)
        for b in range(SHIFT_BITS):
            rolled = pltpu.roll(row, ext_width - (1 << b), 1)
            row = jnp.where(masks[b], rolled, row)
        total = jnp.zeros((rows, width), jnp.float32)
        for k in range(4):
            tap = row if k == 0 else pltpu.roll(row, ext_width - k, 1)
            total = total + w[:, k:k + 1] * tap[:, :width]
        out_ref[t] = total
        top_ref[t] = total[:LAT_HALO]
        bot_ref[t] = total[rows - LAT_HALO:]


def lat_kernel(up_ref, mid_ref, down_ref, d_ref, w_ref, out_ref):
    tracers, rows, width = mid_ref.shape
    ext_rows = rows + 2 * LAT_HALO
    d = d_ref[...]
    w = w_ref[...]
    for t in range(tracers):
        ext = jnp.concatenate([up_ref[t], mid_ref[t], down_ref[t]], axis=0)
        picks = [jnp.zeros((rows, width), jnp.float32) for _ in range(4)]
        for s in range(ext_rows - rows + 1):
            shifted = (ext if s == 0 else pltpu.roll(ext, ext_rows - s, 0))[:rows]
            for k in range(4):
                picks[k] = jnp.where(d[:, k:k + 1] == s, shifted, picks[k])
        total = jnp.zeros((rows, width), jnp.float32)
        for k in range(4):
            total = total + w[:, k:k + 1] * picks[k]
        out_ref[t] = total


def per_device(tracers, lon_offsets, lon_weights, lat_offsets, lat_weights):
    nt, nl, rows, width = tracers.shape
    block = tracers.reshape(nt * nl, rows, width)
    f32 = jnp.float32

    lon_count = lax.axis_size("lon")
    forward = [(i, (i + 1) % lon_count) for i in range(lon_count)]
    backward = [(b, a) for a, b in forward]
    left = lax.ppermute(block[:, :, width - LON_HALO:], "lon", forward)
    right = lax.ppermute(block[:, :, :LON_HALO], "lon", backward)

    base = (LON_HALO - lon_offsets - 1).astype(jnp.int32).reshape(rows, 1)
    lw = jnp.transpose(lon_weights).astype(f32)
    shape = jax.ShapeDtypeStruct((nt * nl, rows, width), f32)
    halo = jax.ShapeDtypeStruct((nt * nl, LAT_HALO, width), f32)
    swept, top, bot = pl.pallas_call(lon_kernel, out_shape=(shape, halo, halo), interpret=INTERPRET)(
        left, block, right, base, lw
    )

    lat_count = lax.axis_size("lat")
    down_pairs = [(i, i + 1) for i in range(lat_count - 1)]
    up_pairs = [(i + 1, i) for i in range(lat_count - 1)]
    up = lax.ppermute(bot, "lat", down_pairs)
    down = lax.ppermute(top, "lat", up_pairs)

    nlat = lat_offsets.shape[0]
    first = lax.axis_index("lat") * rows
    own = first + jnp.arange(rows, dtype=jnp.int32)
    offs = lax.dynamic_slice_in_dim(lat_offsets, first, rows)
    lat_w = lax.dynamic_slice_in_dim(lat_weights, first, rows, axis=1)
    taps = jnp.arange(4, dtype=jnp.int32)
    source = jnp.clip(own[:, None] - offs[:, None] - 1 + taps[None, :], 0, nlat - 1)
    d = (source - first + LAT_HALO - jnp.arange(rows, dtype=jnp.int32)[:, None]).astype(jnp.int32)
    out = pl.pallas_call(lat_kernel, out_shape=shape, interpret=INTERPRET)(
        up, swept, down, d, jnp.transpose(lat_w).astype(f32)
    )
    return out.reshape(tracers.shape)


def solution(mesh):
    return jax.shard_map(
        per_device,
        mesh=mesh,
        in_specs=(P(None, None, "lat", "lon"), P("lat"), P(None, "lat"), P(), P()),
        out_specs=P(None, None, "lat", "lon"),
        check_vma=False,
    )
```

```python
import jax
import jax.numpy as jnp
from jax import lax
from jax.experimental import pallas as pl
from jax.experimental.pallas import tpu as pltpu
from jax.sharding import PartitionSpec as P

LON_HALO = 256
LAT_HALO = 8
SHIFT_BITS = 9
INTERPRET = False


def lon_kernel(left_ref, mid_ref, right_ref, base_ref, w_ref, out_ref, top_ref, bot_ref):
    tracers, rows, width = mid_ref.shape
    ext_width = width + 2 * LON_HALO
    base = base_ref[...]
    masks = [((base >> b) & 1) == 1 for b in range(SHIFT_BITS)]
    w = w_ref[...]
    for t in range(tracers):
        row = jnp.concatenate(
            [left_ref[t, :, width - LON_HALO:], mid_ref[t], right_ref[t, :, :LON_HALO]], axis=1
        )
        for b in range(SHIFT_BITS):
            rolled = pltpu.roll(row, ext_width - (1 << b), 1)
            row = jnp.where(masks[b], rolled, row)
        total = jnp.zeros((rows, width), jnp.float32)
        for k in range(4):
            tap = row if k == 0 else pltpu.roll(row, ext_width - k, 1)
            total = total + w[:, k:k + 1] * tap[:, :width]
        out_ref[t] = total
        top_ref[t] = total[:LAT_HALO]
        bot_ref[t] = total[rows - LAT_HALO:]


def lat_kernel(up_ref, mid_ref, down_ref, d_ref, w_ref, out_ref):
    tracers, rows, width = mid_ref.shape
    ext_rows = rows + 2 * LAT_HALO
    d = d_ref[...]
    w = w_ref[...]
    for t in range(tracers):
        ext = jnp.concatenate([up_ref[t], mid_ref[t], down_ref[t]], axis=0)
        picks = [jnp.zeros((rows, width), jnp.float32) for _ in range(4)]
        for s in range(ext_rows - rows + 1):
            shifted = (ext if s == 0 else pltpu.roll(ext, ext_rows - s, 0))[:rows]
            for k in range(4):
                picks[k] = jnp.where(d[:, k:k + 1] == s, shifted, picks[k])
        total = jnp.zeros((rows, width), jnp.float32)
        for k in range(4):
            total = total + w[:, k:k + 1] * picks[k]
        out_ref[t] = total


def vmem_call(kernel, out_shape, count):
    spec = pl.BlockSpec(memory_space=pltpu.VMEM)
    outs = jax.tree_util.tree_map(lambda _: spec, out_shape)
    return pl.pallas_call(
        kernel, out_shape=out_shape, in_specs=[spec] * count, out_specs=outs, interpret=INTERPRET
    )


def per_device(tracers, lon_offsets, lon_weights, lat_offsets, lat_weights):
    nt, nl, rows, width = tracers.shape
    block = tracers.reshape(nt * nl, rows, width)
    f32 = jnp.float32

    lon_count = lax.axis_size("lon")
    forward = [(i, (i + 1) % lon_count) for i in range(lon_count)]
    backward = [(b, a) for a, b in forward]
    left = lax.ppermute(block, "lon", forward)
    right = lax.ppermute(block, "lon", backward)

    base = (LON_HALO - lon_offsets - 1).astype(jnp.int32).reshape(rows, 1)
    lw = jnp.transpose(lon_weights).astype(f32)
    shape = jax.ShapeDtypeStruct((nt * nl, rows, width), f32)
    halo = jax.ShapeDtypeStruct((nt * nl, LAT_HALO, width), f32)
    swept, top, bot = vmem_call(lon_kernel, (shape, halo, halo), 5)(
        left, block, right, base, lw
    )

    lat_count = lax.axis_size("lat")
    down_pairs = [(i, i + 1) for i in range(lat_count - 1)]
    up_pairs = [(i + 1, i) for i in range(lat_count - 1)]
    up = lax.ppermute(bot, "lat", down_pairs)
    down = lax.ppermute(top, "lat", up_pairs)

    nlat = lat_offsets.shape[0]
    first = lax.axis_index("lat") * rows
    own = first + jnp.arange(rows, dtype=jnp.int32)
    offs = lax.dynamic_slice_in_dim(lat_offsets, first, rows)
    lat_w = lax.dynamic_slice_in_dim(lat_weights, first, rows, axis=1)
    taps = jnp.arange(4, dtype=jnp.int32)
    source = jnp.clip(own[:, None] - offs[:, None] - 1 + taps[None, :], 0, nlat - 1)
    d = (source - first + LAT_HALO - jnp.arange(rows, dtype=jnp.int32)[:, None]).astype(jnp.int32)
    out = vmem_call(lat_kernel, shape, 5)(
        up, swept, down, d, jnp.transpose(lat_w).astype(f32)
    )
    return out.reshape(tracers.shape)


def solution(mesh):
    return jax.shard_map(
        per_device,
        mesh=mesh,
        in_specs=(P(None, None, "lat", "lon"), P("lat"), P(None, "lat"), P(), P()),
        out_specs=P(None, None, "lat", "lon"),
        check_vma=False,
    )
```

```python
import jax
import jax.numpy as jnp
from jax import lax
from jax.experimental import pallas as pl
from jax.experimental.pallas import tpu as pltpu
from jax.sharding import PartitionSpec as P

LON_HALO = 192
LAT_HALO = 8
SHIFT_BITS = 9
INTERPRET = False


def lon_kernel(ext_ref, base_ref, w_ref, out_ref, top_ref, bot_ref):
    tracers, rows, width = out_ref.shape
    ext_width = ext_ref.shape[2]
    base = base_ref[...]
    masks = [((base >> b) & 1) == 1 for b in range(SHIFT_BITS)]
    w = w_ref[...]
    for t in range(tracers):
        row = ext_ref[t]
        for b in range(SHIFT_BITS):
            rolled = pltpu.roll(row, ext_width - (1 << b), 1)
            row = jnp.where(masks[b], rolled, row)
        total = jnp.zeros((rows, width), jnp.float32)
        for k in range(4):
            tap = row if k == 0 else pltpu.roll(row, ext_width - k, 1)
            total = total + w[:, k:k + 1] * tap[:, :width]
        out_ref[t] = total
        top_ref[t] = total[:LAT_HALO]
        bot_ref[t] = total[rows - LAT_HALO:]


def lat_kernel(up_ref, mid_ref, down_ref, d_ref, w_ref, out_ref):
    tracers, rows, width = mid_ref.shape
    ext_rows = rows + 2 * LAT_HALO
    d = d_ref[...]
    w = w_ref[...]
    for t in range(tracers):
        ext = jnp.concatenate([up_ref[t], mid_ref[t], down_ref[t]], axis=0)
        picks = [jnp.zeros((rows, width), jnp.float32) for _ in range(4)]
        for s in range(ext_rows - rows + 1):
            shifted = (ext if s == 0 else pltpu.roll(ext, ext_rows - s, 0))[:rows]
            for k in range(4):
                picks[k] = jnp.where(d[:, k:k + 1] == s, shifted, picks[k])
        total = jnp.zeros((rows, width), jnp.float32)
        for k in range(4):
            total = total + w[:, k:k + 1] * picks[k]
        out_ref[t] = total


def vmem_call(kernel, out_shape, count):
    spec = pl.BlockSpec(memory_space=pltpu.VMEM)
    outs = jax.tree_util.tree_map(lambda _: spec, out_shape)
    return pl.pallas_call(
        kernel, out_shape=out_shape, in_specs=[spec] * count, out_specs=outs, interpret=INTERPRET
    )


def per_device(tracers, lon_offsets, lon_weights, lat_offsets, lat_weights):
    nt, nl, rows, width = tracers.shape
    block = tracers.reshape(nt * nl, rows, width)
    f32 = jnp.float32

    lon_count = lax.axis_size("lon")
    forward = [(i, (i + 1) % lon_count) for i in range(lon_count)]
    backward = [(b, a) for a, b in forward]
    left = lax.ppermute(block[:, :, width - LON_HALO:], "lon", forward)
    right = lax.ppermute(block[:, :, :LON_HALO], "lon", backward)
    ext = jnp.concatenate([left, block, right], axis=2)

    base = (LON_HALO - lon_offsets - 1).astype(jnp.int32).reshape(rows, 1)
    lw = jnp.transpose(lon_weights).astype(f32)
    shape = jax.ShapeDtypeStruct((nt * nl, rows, width), f32)
    halo = jax.ShapeDtypeStruct((nt * nl, LAT_HALO, width), f32)
    swept, top, bot = vmem_call(lon_kernel, (shape, halo, halo), 3)(ext, base, lw)

    lat_count = lax.axis_size("lat")
    down_pairs = [(i, i + 1) for i in range(lat_count - 1)]
    up_pairs = [(i + 1, i) for i in range(lat_count - 1)]
    up = lax.ppermute(bot, "lat", down_pairs)
    down = lax.ppermute(top, "lat", up_pairs)

    nlat = lat_offsets.shape[0]
    first = lax.axis_index("lat") * rows
    own = first + jnp.arange(rows, dtype=jnp.int32)
    offs = lax.dynamic_slice_in_dim(lat_offsets, first, rows)
    lat_w = lax.dynamic_slice_in_dim(lat_weights, first, rows, axis=1)
    taps = jnp.arange(4, dtype=jnp.int32)
    source = jnp.clip(own[:, None] - offs[:, None] - 1 + taps[None, :], 0, nlat - 1)
    d = (source - first + LAT_HALO - jnp.arange(rows, dtype=jnp.int32)[:, None]).astype(jnp.int32)
    out = vmem_call(lat_kernel, shape, 5)(
        up, swept, down, d, jnp.transpose(lat_w).astype(f32)
    )
    return out.reshape(tracers.shape)


def solution(mesh):
    return jax.shard_map(
        per_device,
        mesh=mesh,
        in_specs=(P(None, None, "lat", "lon"), P("lat"), P(None, "lat"), P(), P()),
        out_specs=P(None, None, "lat", "lon"),
        check_vma=False,
    )
```

```python
import jax
import jax.numpy as jnp
from jax import lax
from jax.experimental import pallas as pl
from jax.experimental.pallas import tpu as pltpu
from jax.sharding import PartitionSpec as P

LON_HALO = 256
LAT_HALO = 8
SHIFT_BITS = 9
INTERPRET = False


def row_columns(rows, values):
    row_id = lax.broadcasted_iota(jnp.int32, (rows, 1), 0)
    cols = None
    for j in range(rows):
        here = values(j)
        if cols is None:
            cols = [jnp.full((rows, 1), v, v.dtype) for v in here]
        else:
            cols = [jnp.where(row_id == j, v, c) for v, c in zip(here, cols)]
    return cols


def rotate_rows(row, amount, bits, left):
    width = row.shape[1]
    for b in range(bits):
        step = (width - (1 << b)) if left else (1 << b)
        row = jnp.where(((amount >> b) & 1) == 1, pltpu.roll(row, step, 1), row)
    return row


def pack_kernel(mid_ref, offs_ref, out_ref):
    tracers, rows, width = mid_ref.shape
    need = row_columns(rows, lambda j: [jnp.clip(offs_ref[j] + 1, 0, LON_HALO)])[0]
    for t in range(tracers):
        block = mid_ref[t]
        window = jnp.concatenate(
            [block[:, width - LON_HALO:], block[:, :LON_HALO]], axis=1
        )
        out_ref[t] = rotate_rows(window, LON_HALO - need, SHIFT_BITS, True)[:, :LON_HALO]


def lon_kernel(p_ref, mid_ref, q_ref, par_ref, offs_ref, lw_ref, out_ref, top_ref, bot_ref):
    tracers, rows, width = mid_ref.shape
    ext_width = width + 2 * LON_HALO
    even_lon = par_ref[...] == 0
    cols = row_columns(
        rows,
        lambda j: [LON_HALO - offs_ref[j] - 1, jnp.clip(offs_ref[j] + 1, 0, LON_HALO)]
        + [lw_ref[k, j] for k in range(4)],
    )
    base, need, w = cols[0], cols[1], cols[2:]
    halo_bits = LON_HALO.bit_length() - 1
    masks = [((base >> b) & 1) == 1 for b in range(SHIFT_BITS)]
    for t in range(tracers):
        p, q = p_ref[t], q_ref[t]
        left = rotate_rows(jnp.where(even_lon, q, p), (LON_HALO - need) % LON_HALO, halo_bits, False)
        right = rotate_rows(jnp.where(even_lon, p, q), need, halo_bits, True)
        row = jnp.concatenate([left, mid_ref[t], right], axis=1)
        for b in range(SHIFT_BITS):
            rolled = pltpu.roll(row, ext_width - (1 << b), 1)
            row = jnp.where(masks[b], rolled, row)
        total = jnp.zeros((rows, width), jnp.float32)
        for k in range(4):
            tap = row if k == 0 else pltpu.roll(row, ext_width - k, 1)
            total = total + w[k] * tap[:, :width]
        out_ref[t] = total
        top_ref[t] = total[:LAT_HALO]
        bot_ref[t] = total[rows - LAT_HALO:]


def lat_kernel(up_ref, mid_ref, down_ref, first_ref, offs_ref, lw_ref, out_ref):
    tracers, rows, width = mid_ref.shape
    ext_rows = rows + 2 * LAT_HALO
    nlat = offs_ref.shape[0]
    first = first_ref[0]

    def values(j):
        row = first + j
        shift = offs_ref[row]
        picks = [jnp.clip(row - shift - 1 + k, 0, nlat - 1) - first + LAT_HALO - j for k in range(4)]
        return picks + [lw_ref[k, row] for k in range(4)]

    cols = row_columns(rows, values)
    d, w = cols[:4], cols[4:]
    for t in range(tracers):
        ext = jnp.concatenate([up_ref[t], mid_ref[t], down_ref[t]], axis=0)
        picks = [jnp.zeros((rows, width), jnp.float32) for _ in range(4)]
        for s in range(ext_rows - rows + 1):
            shifted = (ext if s == 0 else pltpu.roll(ext, ext_rows - s, 0))[:rows]
            for k in range(4):
                picks[k] = jnp.where(d[k] == s, shifted, picks[k])
        total = jnp.zeros((rows, width), jnp.float32)
        for k in range(4):
            total = total + w[k] * picks[k]
        out_ref[t] = total


def call(kernel, out_shape, spaces):
    return pl.pallas_call(
        kernel,
        out_shape=out_shape,
        in_specs=[pl.BlockSpec(memory_space=m) for m in spaces],
        interpret=INTERPRET,
    )


def per_device(tracers, lon_offsets, lon_weights, lat_offsets, lat_weights):
    nt, nl, rows, width = tracers.shape
    block = tracers.reshape(nt * nl, rows, width)
    f32 = jnp.float32

    lon_count = lax.axis_size("lon")
    f32 = jnp.float32
    offs = lon_offsets.astype(jnp.int32)
    vmem, smem = pltpu.VMEM, pltpu.SMEM
    packed_shape = jax.ShapeDtypeStruct((nt * nl, rows, LON_HALO), f32)
    packed = call(pack_kernel, packed_shape, [vmem, smem])(block, offs)
    partner = lax.ppermute(packed, "lon", [(i, i ^ 1) for i in range(lon_count)])
    onward = [(i, (i + 2) % lon_count if i % 2 == 0 else (i - 2) % lon_count) for i in range(lon_count)]
    relayed = lax.ppermute(partner, "lon", onward)
    par = (lax.axis_index("lon") % 2).astype(jnp.int32).reshape(1, 1)

    shape = jax.ShapeDtypeStruct((nt * nl, rows, width), f32)
    halo = jax.ShapeDtypeStruct((nt * nl, LAT_HALO, width), f32)
    swept, top, bot = call(lon_kernel, (shape, halo, halo), [vmem] * 4 + [smem] * 2)(
        partner, block, relayed, par, offs, lon_weights.astype(f32)
    )

    lat_count = lax.axis_size("lat")
    down_pairs = [(i, i + 1) for i in range(lat_count - 1)]
    up_pairs = [(i + 1, i) for i in range(lat_count - 1)]
    up = lax.ppermute(bot, "lat", down_pairs)
    down = lax.ppermute(top, "lat", up_pairs)

    first = (lax.axis_index("lat") * rows).astype(jnp.int32).reshape(1)
    out = call(lat_kernel, shape, [vmem] * 3 + [smem] * 3)(
        up, swept, down, first, lat_offsets.astype(jnp.int32), lat_weights.astype(f32)
    )
    return out.reshape(tracers.shape)


def solution(mesh):
    return jax.shard_map(
        per_device,
        mesh=mesh,
        in_specs=(P(None, None, "lat", "lon"), P("lat"), P(None, "lat"), P(), P()),
        out_specs=P(None, None, "lat", "lon"),
        check_vma=False,
    )
```

```python
import jax
import jax.numpy as jnp
from jax import lax
from jax.experimental import pallas as pl
from jax.experimental.pallas import tpu as pltpu
from jax.sharding import PartitionSpec as P

LON_HALO = 256
LAT_HALO = 8
SHIFT_BITS = 9
PACK_SHIFT = 64
INTERPRET = False


def row_columns(rows, values):
    row_id = lax.broadcasted_iota(jnp.int32, (rows, 1), 0)
    cols = None
    for j in range(rows):
        here = values(j)
        if cols is None:
            cols = [jnp.full((rows, 1), v, v.dtype) for v in here]
        else:
            cols = [jnp.where(row_id == j, v, c) for v, c in zip(here, cols)]
    return cols


def rotate_rows(row, amount, bits, left):
    width = row.shape[1]
    for b in range(bits):
        step = (width - (1 << b)) if left else (1 << b)
        row = jnp.where(((amount >> b) & 1) == 1, pltpu.roll(row, step, 1), row)
    return row


def lon_kernel(p_ref, mid_ref, q_ref, par_ref, offs_ref, lw_ref, out_ref, top_ref, bot_ref):
    tracers, rows, width = mid_ref.shape
    ext_width = width + 2 * LON_HALO
    even_lon = par_ref[...] == 0
    cols = row_columns(
        rows,
        lambda j: [LON_HALO - offs_ref[j] - 1, jnp.clip(offs_ref[j] + 1, 0, LON_HALO)]
        + [lw_ref[k, j] for k in range(4)],
    )
    base, need, w = cols[0], cols[1], cols[2:]
    ahead = need > 0
    masks = [((base >> b) & 1) == 1 for b in range(SHIFT_BITS)]
    for t in range(tracers):
        p, q = p_ref[t], q_ref[t]
        left = pltpu.roll(jnp.where(even_lon, q, p), PACK_SHIFT, 1)
        right = jnp.where(even_lon, p, q)
        right = jnp.where(ahead, pltpu.roll(right, PACK_SHIFT, 1), right)
        row = jnp.concatenate([left, mid_ref[t], right], axis=1)
        for b in range(SHIFT_BITS):
            rolled = pltpu.roll(row, ext_width - (1 << b), 1)
            row = jnp.where(masks[b], rolled, row)
        total = jnp.zeros((rows, width), jnp.float32)
        for k in range(4):
            tap = row if k == 0 else pltpu.roll(row, ext_width - k, 1)
            total = total + w[k] * tap[:, :width]
        out_ref[t] = total
        top_ref[t] = total[:LAT_HALO]
        bot_ref[t] = total[rows - LAT_HALO:]


def lat_kernel(up_ref, mid_ref, down_ref, first_ref, offs_ref, lw_ref, out_ref):
    tracers, rows, width = mid_ref.shape
    ext_rows = rows + 2 * LAT_HALO
    nlat = offs_ref.shape[0]
    first = first_ref[0]

    def values(j):
        row = first + j
        shift = offs_ref[row]
        picks = [jnp.clip(row - shift - 1 + k, 0, nlat - 1) - first + LAT_HALO - j for k in range(4)]
        return picks + [lw_ref[k, row] for k in range(4)]

    cols = row_columns(rows, values)
    d, w = cols[:4], cols[4:]
    for t in range(tracers):
        ext = jnp.concatenate([up_ref[t], mid_ref[t], down_ref[t]], axis=0)
        picks = [jnp.zeros((rows, width), jnp.float32) for _ in range(4)]
        for s in range(ext_rows - rows + 1):
            shifted = (ext if s == 0 else pltpu.roll(ext, ext_rows - s, 0))[:rows]
            for k in range(4):
                picks[k] = jnp.where(d[k] == s, shifted, picks[k])
        total = jnp.zeros((rows, width), jnp.float32)
        for k in range(4):
            total = total + w[k] * picks[k]
        out_ref[t] = total


def call(kernel, out_shape, spaces):
    return pl.pallas_call(
        kernel,
        out_shape=out_shape,
        in_specs=[pl.BlockSpec(memory_space=m) for m in spaces],
        interpret=INTERPRET,
    )


def per_device(tracers, lon_offsets, lon_weights, lat_offsets, lat_weights):
    nt, nl, rows, width = tracers.shape
    block = tracers.reshape(nt * nl, rows, width)
    f32 = jnp.float32

    lon_count = lax.axis_size("lon")
    f32 = jnp.float32
    offs = lon_offsets.astype(jnp.int32)
    vmem, smem = pltpu.VMEM, pltpu.SMEM
    tail = width - LON_HALO + PACK_SHIFT
    ahead = (offs >= 0)[None, :, None]
    packed = jnp.where(
        ahead,
        jnp.concatenate([block[:, :, tail:], block[:, :, :LON_HALO - width + tail]], axis=2),
        block[:, :, :LON_HALO],
    )
    partner = lax.ppermute(packed, "lon", [(i, i ^ 1) for i in range(lon_count)])
    onward = [(i, (i + 2) % lon_count if i % 2 == 0 else (i - 2) % lon_count) for i in range(lon_count)]
    relayed = lax.ppermute(partner, "lon", onward)
    par = (lax.axis_index("lon") % 2).astype(jnp.int32).reshape(1, 1)

    shape = jax.ShapeDtypeStruct((nt * nl, rows, width), f32)
    halo = jax.ShapeDtypeStruct((nt * nl, LAT_HALO, width), f32)
    swept, top, bot = call(lon_kernel, (shape, halo, halo), [vmem] * 4 + [smem] * 2)(
        partner, block, relayed, par, offs, lon_weights.astype(f32)
    )

    lat_count = lax.axis_size("lat")
    down_pairs = [(i, i + 1) for i in range(lat_count - 1)]
    up_pairs = [(i + 1, i) for i in range(lat_count - 1)]
    up = lax.ppermute(bot, "lat", down_pairs)
    down = lax.ppermute(top, "lat", up_pairs)

    first = (lax.axis_index("lat") * rows).astype(jnp.int32).reshape(1)
    out = call(lat_kernel, shape, [vmem] * 3 + [smem] * 3)(
        up, swept, down, first, lat_offsets.astype(jnp.int32), lat_weights.astype(f32)
    )
    return out.reshape(tracers.shape)


def solution(mesh):
    return jax.shard_map(
        per_device,
        mesh=mesh,
        in_specs=(P(None, None, "lat", "lon"), P("lat"), P(None, "lat"), P(), P()),
        out_specs=P(None, None, "lat", "lon"),
        check_vma=False,
    )
```

```python
import jax
import jax.numpy as jnp
from jax import lax
from jax.experimental import pallas as pl
from jax.experimental.pallas import tpu as pltpu
from jax.sharding import PartitionSpec as P

LON_HALO = 256
LAT_HALO = 8
SHIFT_BITS = 9
PACK_SHIFT = 64
INTERPRET = False


def row_columns(rows, values):
    row_id = lax.broadcasted_iota(jnp.int32, (rows, 1), 0)
    cols = None
    for j in range(rows):
        here = values(j)
        if cols is None:
            cols = [jnp.full((rows, 1), v, v.dtype) for v in here]
        else:
            cols = [jnp.where(row_id == j, v, c) for v, c in zip(here, cols)]
    return cols


def rotate_rows(row, amount, bits, left):
    width = row.shape[1]
    for b in range(bits):
        step = (width - (1 << b)) if left else (1 << b)
        row = jnp.where(((amount >> b) & 1) == 1, pltpu.roll(row, step, 1), row)
    return row


def lon_kernel(p_ref, mid_ref, q_ref, par_ref, offs_ref, lw_ref, out_ref, top_ref, bot_ref):
    tracers, rows, width = mid_ref.shape
    ext_width = width + 2 * LON_HALO
    even_lon = par_ref[...] == 0
    base = offs_ref[...]
    w = [lw_ref[:, k:k + 1] for k in range(4)]
    ahead = base < LON_HALO
    masks = [((base >> b) & 1) == 1 for b in range(SHIFT_BITS)]
    for t in range(tracers):
        p, q = p_ref[t], q_ref[t]
        left = pltpu.roll(jnp.where(even_lon, q, p), PACK_SHIFT, 1)
        right = jnp.where(even_lon, p, q)
        right = jnp.where(ahead, pltpu.roll(right, PACK_SHIFT, 1), right)
        row = jnp.concatenate([left, mid_ref[t], right], axis=1)
        for b in range(SHIFT_BITS):
            rolled = pltpu.roll(row, ext_width - (1 << b), 1)
            row = jnp.where(masks[b], rolled, row)
        total = jnp.zeros((rows, width), jnp.float32)
        for k in range(4):
            tap = row if k == 0 else pltpu.roll(row, ext_width - k, 1)
            total = total + w[k] * tap[:, :width]
        out_ref[t] = total
        top_ref[t] = total[:LAT_HALO]
        bot_ref[t] = total[rows - LAT_HALO:]


def lat_kernel(up_ref, mid_ref, down_ref, offs_ref, lw_ref, out_ref):
    tracers, rows, width = mid_ref.shape
    ext_rows = rows + 2 * LAT_HALO
    d = [offs_ref[:, k:k + 1] for k in range(4)]
    w = [lw_ref[:, k:k + 1] for k in range(4)]
    for t in range(tracers):
        ext = jnp.concatenate([up_ref[t], mid_ref[t], down_ref[t]], axis=0)
        picks = [jnp.zeros((rows, width), jnp.float32) for _ in range(4)]
        for s in range(LAT_HALO - 5, LAT_HALO + 7):
            shifted = pltpu.roll(ext, ext_rows - s, 0)[:rows]
            for k in range(4):
                picks[k] = jnp.where(d[k] == s, shifted, picks[k])
        total = jnp.zeros((rows, width), jnp.float32)
        for k in range(4):
            total = total + w[k] * picks[k]
        out_ref[t] = total


def call(kernel, out_shape, spaces):
    return pl.pallas_call(
        kernel,
        out_shape=out_shape,
        in_specs=[pl.BlockSpec(memory_space=m) for m in spaces],
        interpret=INTERPRET,
    )


def per_device(tracers, lon_offsets, lon_weights, lat_offsets, lat_weights):
    nt, nl, rows, width = tracers.shape
    block = tracers.reshape(nt * nl, rows, width)
    f32 = jnp.float32

    lon_count = lax.axis_size("lon")
    f32 = jnp.float32
    offs = lon_offsets.astype(jnp.int32)
    vmem, smem = pltpu.VMEM, pltpu.SMEM
    tail = width - LON_HALO + PACK_SHIFT
    ahead = (offs >= 0)[None, :, None]
    packed = jnp.where(
        ahead,
        jnp.concatenate([block[:, :, tail:], block[:, :, :LON_HALO - width + tail]], axis=2),
        block[:, :, :LON_HALO],
    )
    partner = lax.ppermute(packed, "lon", [(i, i ^ 1) for i in range(lon_count)])
    onward = [(i, (i + 2) % lon_count if i % 2 == 0 else (i - 2) % lon_count) for i in range(lon_count)]
    relayed = lax.ppermute(partner, "lon", onward)
    par = (lax.axis_index("lon") % 2).astype(jnp.int32).reshape(1, 1)

    shape = jax.ShapeDtypeStruct((nt * nl, rows, width), f32)
    halo = jax.ShapeDtypeStruct((nt * nl, LAT_HALO, width), f32)
    base = (LON_HALO - offs - 1).reshape(rows, 1)
    lw = jnp.transpose(lon_weights).astype(f32)
    swept, top, bot = call(lon_kernel, (shape, halo, halo), [vmem] * 6)(
        partner, block, relayed, par, base, lw
    )

    lat_count = lax.axis_size("lat")
    down_pairs = [(i, i + 1) for i in range(lat_count - 1)]
    up_pairs = [(i + 1, i) for i in range(lat_count - 1)]
    up = lax.ppermute(bot, "lat", down_pairs)
    down = lax.ppermute(top, "lat", up_pairs)

    nlat = lat_offsets.shape[0]
    first = lax.axis_index("lat") * rows
    own = first + jnp.arange(rows, dtype=jnp.int32)
    lat_offs = lax.dynamic_slice_in_dim(lat_offsets, first, rows)
    lat_w = lax.dynamic_slice_in_dim(lat_weights, first, rows, axis=1)
    taps = jnp.arange(4, dtype=jnp.int32)
    source = jnp.clip(own[:, None] - lat_offs[:, None] - 1 + taps[None, :], 0, nlat - 1)
    d = (source - first + LAT_HALO - jnp.arange(rows, dtype=jnp.int32)[:, None]).astype(jnp.int32)
    out = call(lat_kernel, shape, [vmem] * 5)(
        up, swept, down, d, jnp.transpose(lat_w).astype(f32)
    )
    return out.reshape(tracers.shape)


def solution(mesh):
    return jax.shard_map(
        per_device,
        mesh=mesh,
        in_specs=(P(None, None, "lat", "lon"), P("lat"), P(None, "lat"), P(), P()),
        out_specs=P(None, None, "lat", "lon"),
        check_vma=False,
    )
```

```python
import jax
import jax.numpy as jnp
from jax import lax
from jax.experimental import pallas as pl
from jax.experimental.pallas import tpu as pltpu
from jax.sharding import PartitionSpec as P

LON_HALO = 256
LAT_HALO = 8
SHIFT_BITS = 9
INTERPRET = False


def row_columns(rows, values):
    row_id = lax.broadcasted_iota(jnp.int32, (rows, 1), 0)
    cols = None
    for j in range(rows):
        here = values(j)
        if cols is None:
            cols = [jnp.full((rows, 1), v, v.dtype) for v in here]
        else:
            cols = [jnp.where(row_id == j, v, c) for v, c in zip(here, cols)]
    return cols


def rotate_rows(row, amount, bits, left):
    width = row.shape[1]
    for b in range(bits):
        step = (width - (1 << b)) if left else (1 << b)
        row = jnp.where(((amount >> b) & 1) == 1, pltpu.roll(row, step, 1), row)
    return row


def lon_kernel(p_ref, mid_ref, q_ref, par_ref, offs_ref, lw_ref, out_ref, top_ref, bot_ref):
    tracers, rows, width = mid_ref.shape
    ext_width = width + 2 * LON_HALO
    even_lon = par_ref[...] == 0
    base = offs_ref[...]
    w = [lw_ref[:, k:k + 1] for k in range(4)]
    masks = [((base >> b) & 1) == 1 for b in range(SHIFT_BITS)]
    for t in range(tracers):
        p, q = p_ref[t], q_ref[t]
        left = jnp.where(even_lon, q, p)
        right = jnp.where(even_lon, p, q)
        row = jnp.concatenate([left, mid_ref[t], right], axis=1)
        for b in range(SHIFT_BITS):
            rolled = pltpu.roll(row, ext_width - (1 << b), 1)
            row = jnp.where(masks[b], rolled, row)
        total = jnp.zeros((rows, width), jnp.float32)
        for k in range(4):
            tap = row if k == 0 else pltpu.roll(row, ext_width - k, 1)
            total = total + w[k] * tap[:, :width]
        out_ref[t] = total
        top_ref[t] = total[:LAT_HALO]
        bot_ref[t] = total[rows - LAT_HALO:]


def lat_kernel(up_ref, mid_ref, down_ref, offs_ref, lw_ref, out_ref):
    tracers, rows, width = mid_ref.shape
    ext_rows = rows + 2 * LAT_HALO
    d = [offs_ref[:, k:k + 1] for k in range(4)]
    w = [lw_ref[:, k:k + 1] for k in range(4)]
    for t in range(tracers):
        ext = jnp.concatenate([up_ref[t], mid_ref[t], down_ref[t]], axis=0)
        picks = [jnp.zeros((rows, width), jnp.float32) for _ in range(4)]
        for s in range(LAT_HALO - 5, LAT_HALO + 7):
            shifted = pltpu.roll(ext, ext_rows - s, 0)[:rows]
            for k in range(4):
                picks[k] = jnp.where(d[k] == s, shifted, picks[k])
        total = jnp.zeros((rows, width), jnp.float32)
        for k in range(4):
            total = total + w[k] * picks[k]
        out_ref[t] = total


def call(kernel, out_shape, spaces):
    return pl.pallas_call(
        kernel,
        out_shape=out_shape,
        in_specs=[pl.BlockSpec(memory_space=m) for m in spaces],
        interpret=INTERPRET,
    )


def per_device(tracers, lon_offsets, lon_weights, lat_offsets, lat_weights):
    nt, nl, rows, width = tracers.shape
    block = tracers.reshape(nt * nl, rows, width)
    f32 = jnp.float32

    lon_count = lax.axis_size("lon")
    f32 = jnp.float32
    offs = lon_offsets.astype(jnp.int32)
    vmem, smem = pltpu.VMEM, pltpu.SMEM
    third = width // 3
    lo = jnp.where((offs >= 2)[None, :, None], block[:, :, third:2 * third], block[:, :, :third])
    hi = jnp.where((offs <= -1)[None, :, None], block[:, :, third:2 * third], block[:, :, 2 * third:])
    packed = jnp.concatenate([lo, hi], axis=2)
    partner = lax.ppermute(packed, "lon", [(i, i ^ 1) for i in range(lon_count)])
    onward = [(i, (i + 2) % lon_count if i % 2 == 0 else (i - 2) % lon_count) for i in range(lon_count)]
    relayed = lax.ppermute(partner, "lon", onward)
    par = (lax.axis_index("lon") % 2).astype(jnp.int32).reshape(1, 1)

    shape = jax.ShapeDtypeStruct((nt * nl, rows, width), f32)
    halo = jax.ShapeDtypeStruct((nt * nl, LAT_HALO, width), f32)
    base = (LON_HALO - offs - 1).reshape(rows, 1)
    lw = jnp.transpose(lon_weights).astype(f32)
    swept, top, bot = call(lon_kernel, (shape, halo, halo), [vmem] * 6)(
        partner, block, relayed, par, base, lw
    )

    lat_count = lax.axis_size("lat")
    down_pairs = [(i, i + 1) for i in range(lat_count - 1)]
    up_pairs = [(i + 1, i) for i in range(lat_count - 1)]
    up = lax.ppermute(bot, "lat", down_pairs)
    down = lax.ppermute(top, "lat", up_pairs)

    nlat = lat_offsets.shape[0]
    first = lax.axis_index("lat") * rows
    own = first + jnp.arange(rows, dtype=jnp.int32)
    lat_offs = lax.dynamic_slice_in_dim(lat_offsets, first, rows)
    lat_w = lax.dynamic_slice_in_dim(lat_weights, first, rows, axis=1)
    taps = jnp.arange(4, dtype=jnp.int32)
    source = jnp.clip(own[:, None] - lat_offs[:, None] - 1 + taps[None, :], 0, nlat - 1)
    d = (source - first + LAT_HALO - jnp.arange(rows, dtype=jnp.int32)[:, None]).astype(jnp.int32)
    out = call(lat_kernel, shape, [vmem] * 5)(
        up, swept, down, d, jnp.transpose(lat_w).astype(f32)
    )
    return out.reshape(tracers.shape)


def solution(mesh):
    return jax.shard_map(
        per_device,
        mesh=mesh,
        in_specs=(P(None, None, "lat", "lon"), P("lat"), P(None, "lat"), P(), P()),
        out_specs=P(None, None, "lat", "lon"),
        check_vma=False,
    )
```

```python
import jax
import jax.numpy as jnp
from jax import lax
from jax.experimental import pallas as pl
from jax.experimental.pallas import tpu as pltpu
from jax.sharding import PartitionSpec as P

LON_HALO = 256
LAT_HALO = 8
SHIFT_BITS = 9
INTERPRET = False


def row_columns(rows, values):
    row_id = lax.broadcasted_iota(jnp.int32, (rows, 1), 0)
    cols = None
    for j in range(rows):
        here = values(j)
        if cols is None:
            cols = [jnp.full((rows, 1), v, v.dtype) for v in here]
        else:
            cols = [jnp.where(row_id == j, v, c) for v, c in zip(here, cols)]
    return cols


def rotate_rows(row, amount, bits, left):
    width = row.shape[1]
    for b in range(bits):
        step = (width - (1 << b)) if left else (1 << b)
        row = jnp.where(((amount >> b) & 1) == 1, pltpu.roll(row, step, 1), row)
    return row


def lon_kernel(p_ref, mid_ref, q_ref, par_ref, offs_ref, lw_ref, out_ref, top_ref, bot_ref):
    tracers, rows, width = mid_ref.shape
    ext_width = width + 2 * LON_HALO
    even_lon = par_ref[...] == 0
    base = offs_ref[...]
    w = [lw_ref[:, k:k + 1] for k in range(4)]
    masks = [((base >> b) & 1) == 1 for b in range(SHIFT_BITS)]
    for t in range(tracers):
        p, q = p_ref[t], q_ref[t]
        left = jnp.where(even_lon, q, p)
        right = jnp.where(even_lon, p, q)
        row = jnp.concatenate([left, mid_ref[t], right], axis=1)
        for b in range(SHIFT_BITS):
            rolled = pltpu.roll(row, ext_width - (1 << b), 1)
            row = jnp.where(masks[b], rolled, row)
        total = jnp.zeros((rows, width), jnp.float32)
        for k in range(4):
            tap = row if k == 0 else pltpu.roll(row, ext_width - k, 1)
            total = total + w[k] * tap[:, :width]
        out_ref[t] = total
        top_ref[t] = total[:LAT_HALO]
        bot_ref[t] = total[rows - LAT_HALO:]


def lat_kernel(up_ref, mid_ref, down_ref, coef_ref, out_ref):
    tracers, rows, width = mid_ref.shape
    ext_rows = rows + 2 * LAT_HALO
    coef = coef_ref[...]
    for t in range(tracers):
        ext = jnp.concatenate([up_ref[t], mid_ref[t], down_ref[t]], axis=0)
        total = jnp.zeros((rows, width), jnp.float32)
        for i, s in enumerate(range(LAT_HALO - 5, LAT_HALO + 7)):
            shifted = pltpu.roll(ext, ext_rows - s, 0)[:rows]
            total = total + coef[:, i:i + 1] * shifted
        out_ref[t] = total


def call(kernel, out_shape, spaces):
    return pl.pallas_call(
        kernel,
        out_shape=out_shape,
        in_specs=[pl.BlockSpec(memory_space=m) for m in spaces],
        interpret=INTERPRET,
    )


def per_device(tracers, lon_offsets, lon_weights, lat_offsets, lat_weights):
    nt, nl, rows, width = tracers.shape
    block = tracers.reshape(nt * nl, rows, width)
    f32 = jnp.float32

    lon_count = lax.axis_size("lon")
    f32 = jnp.float32
    offs = lon_offsets.astype(jnp.int32)
    vmem, smem = pltpu.VMEM, pltpu.SMEM
    third = width // 3
    lo = jnp.where((offs >= 2)[None, :, None], block[:, :, third:2 * third], block[:, :, :third])
    hi = jnp.where((offs <= -1)[None, :, None], block[:, :, third:2 * third], block[:, :, 2 * third:])
    packed = jnp.concatenate([lo, hi], axis=2)
    partner = lax.ppermute(packed, "lon", [(i, i ^ 1) for i in range(lon_count)])
    onward = [(i, (i + 2) % lon_count if i % 2 == 0 else (i - 2) % lon_count) for i in range(lon_count)]
    relayed = lax.ppermute(partner, "lon", onward)
    par = (lax.axis_index("lon") % 2).astype(jnp.int32).reshape(1, 1)

    shape = jax.ShapeDtypeStruct((nt * nl, rows, width), f32)
    halo = jax.ShapeDtypeStruct((nt * nl, LAT_HALO, width), f32)
    base = (LON_HALO - offs - 1).reshape(rows, 1)
    lw = jnp.transpose(lon_weights).astype(f32)
    swept, top, bot = call(lon_kernel, (shape, halo, halo), [vmem] * 6)(
        partner, block, relayed, par, base, lw
    )

    lat_count = lax.axis_size("lat")
    down_pairs = [(i, i + 1) for i in range(lat_count - 1)]
    up_pairs = [(i + 1, i) for i in range(lat_count - 1)]
    up = lax.ppermute(bot, "lat", down_pairs)
    down = lax.ppermute(top, "lat", up_pairs)

    nlat = lat_offsets.shape[0]
    first = lax.axis_index("lat") * rows
    own = first + jnp.arange(rows, dtype=jnp.int32)
    lat_offs = lax.dynamic_slice_in_dim(lat_offsets, first, rows)
    lat_w = lax.dynamic_slice_in_dim(lat_weights, first, rows, axis=1)
    taps = jnp.arange(4, dtype=jnp.int32)
    source = jnp.clip(own[:, None] - lat_offs[:, None] - 1 + taps[None, :], 0, nlat - 1)
    d = (source - first + LAT_HALO - jnp.arange(rows, dtype=jnp.int32)[:, None]).astype(jnp.int32)
    shifts = jnp.arange(LAT_HALO - 5, LAT_HALO + 7, dtype=jnp.int32)
    hits = (d[:, :, None] == shifts[None, None, :]).astype(f32)
    coef = jnp.einsum("jk,jks->js", jnp.transpose(lat_w).astype(f32), hits,
                      precision=lax.Precision.HIGHEST)
    out = call(lat_kernel, shape, [vmem] * 4)(up, swept, down, coef)
    return out.reshape(tracers.shape)


def solution(mesh):
    return jax.shard_map(
        per_device,
        mesh=mesh,
        in_specs=(P(None, None, "lat", "lon"), P("lat"), P(None, "lat"), P(), P()),
        out_specs=P(None, None, "lat", "lon"),
        check_vma=False,
    )
```
